256 devices in a mesh: row: 16 (over x_hi, y, core), col: 16 (over z, x_lo).
Axes of the slice: x: 4 (x_hi: 2, x_lo: 2; x = x_hi * 2 + x_lo), y: 4, z: 8, core: 2. Of those that a mesh axis runs over, the one named last changes fastest.
Arguments:
- stem: bfloat16 [16, 16, 1, 512, 2, 512], P('row', 'col'), may hold values from -6 to 6
- branch: bfloat16 [16, 4, 2, 512, 512], P('row', None, None, None, 'col'), may hold values from -0.1875 to 0.1875
Outputs:
- amplitudes: bfloat16 [16, 16, 1, 512, 2, 512], P('row', 'col')
The draws below stay inside these ranges and needn't reach their ends.
All inputs are finite; a program needn't handle non-finite values.
Results may differ from the reference program's by a relative error of at most 0.0075.
Values may be sent and summed in bfloat16 or wider, within the bound.
No kernel may reach another device: no remote copies, remote signals or barrier semaphores. Data moves between devices by JAX's collectives and lax.ppermute only.
A program may use at most 64 MiB of HBM per device.

```python
import jax
import jax.numpy as jnp
from jax import lax

ORDER = 512
STEM_ROWS = 1
BUILDS = 4
N_ROW = 16
N_COL = 16


def levels(key, dims, split, least, largest):
    def one(axis_at, parts):
        steps = jax.random.uniform(jax.random.fold_in(jax.random.fold_in(key, 6), axis_at), (parts,), jnp.float32, least / len(split), largest / len(split))
        return jnp.repeat(jnp.exp(steps), dims[axis_at] // parts).reshape((-1,) + (1,) * (len(dims) - axis_at - 1))

    level = one(*split[0])
    for cut in split[1:]:
        level = level * one(*cut)
    return level


def gaussian(own_key, shape, width, limit, cuts=(), held_as=jnp.bfloat16):
    values = jax.random.normal(own_key, shape, jnp.float32) * width
    if len(cuts) > 0:
        values = levels(own_key, shape, cuts, -0.22, 0.18) * values
    return jnp.clip(values, min=-limit, max=limit).astype(held_as)


def setup_inputs(seed: int = 0) -> dict:
    streams_of = jax.random.split(jax.random.key(seed), 3)
    return {
        "stem": gaussian(streams_of[0], (N_ROW, N_COL, STEM_ROWS, ORDER, 2, ORDER), 1.0, 6.0, ((0, 16), (1, 16))),
        "branch": gaussian(streams_of[1], (N_ROW, BUILDS, 2, ORDER, ORDER), (2 * ORDER) ** -0.5, 0.1875, ((0, 16), (4, 16))),
    }


def product_right(left, right):
    return jnp.einsum("...j,kj->...k", left, right, precision=lax.Precision.HIGHEST)


def product_left(left, right):
    return jnp.einsum("ki,...ij->...kj", left, right, precision=lax.Precision.HIGHEST)


def right_apply(block, branch_one):
    real_in = block[..., 0, :].astype(jnp.float32)
    imag_in = block[..., 1, :].astype(jnp.float32)
    real_w = branch_one[0].astype(jnp.float32)
    imag_w = branch_one[1].astype(jnp.float32)
    real_out = product_right(real_in, real_w) - product_right(imag_in, imag_w)
    imag_out = product_right(real_in, imag_w) + product_right(imag_in, real_w)
    return jnp.stack([real_out, imag_out], axis=-2).astype(jnp.bfloat16)


def left_apply(block, branch_one):
    real_in = block[..., :, 0, :].astype(jnp.float32)
    imag_in = block[..., :, 1, :].astype(jnp.float32)
    real_w = branch_one[0].astype(jnp.float32)
    imag_w = branch_one[1].astype(jnp.float32)
    real_out = product_left(real_w, real_in) - product_left(imag_w, imag_in)
    imag_out = product_left(imag_w, real_in) + product_left(real_w, imag_in)
    return jnp.stack([real_out, imag_out], axis=-2).astype(jnp.bfloat16)


def reference(stem, branch):
    row_count = stem.shape[0]
    col_count = stem.shape[1]
    slab_count = stem.shape[2]
    order_size = stem.shape[3]

    def first_step(packed):
        block, branch_row = packed
        return left_apply(right_apply(block, branch_row[1]), branch_row[0])

    step_first = lax.map(first_step, (stem, branch))
    share = order_size // row_count
    moved = step_first.reshape(row_count, col_count, slab_count, row_count, share, 2, order_size)
    moved = jnp.transpose(moved, (3, 1, 2, 0, 4, 5, 6)).reshape(stem.shape)

    def second_step(packed):
        block, branch_row = packed
        return left_apply(right_apply(block, branch_row[3]), branch_row[2])

    step_second = lax.map(second_step, (moved, branch))
    final = step_second.reshape(row_count, col_count, slab_count, order_size, 2, row_count, share)
    final = jnp.transpose(final, (5, 1, 2, 3, 4, 0, 6)).reshape(stem.shape)
    return final
```

```python
import jax
import jax.numpy as jnp
from jax import lax
from jax.sharding import Mesh
from jax.sharding import PartitionSpec as P


def right_piece(block, piece_t):
    items = block.shape[0]
    order_size = block.shape[1]
    flat = block.reshape(items * order_size, 2 * order_size)
    real_t = piece_t[0]
    imag_t = piece_t[1]
    weight = jnp.block([[real_t, imag_t], [-imag_t, real_t]])
    product = jnp.dot(flat, weight, preferred_element_type=jnp.float32)
    return product.reshape(items, order_size, 2, order_size)


def left_piece(block, piece_t):
    rows_out = piece_t.shape[2]
    real_in = block[:, :, 0, :]
    imag_in = block[:, :, 1, :]
    real_w = piece_t[0]
    imag_w = piece_t[1]
    weight_real = jnp.concatenate([real_w, imag_w], axis=1)
    weight_imag = jnp.concatenate([-imag_w, real_w], axis=1)
    product = jnp.einsum("ix,eij->exj", weight_real, real_in, preferred_element_type=jnp.float32)
    product = product + jnp.einsum(
        "ix,eij->exj", weight_imag, imag_in, preferred_element_type=jnp.float32
    )
    return jnp.stack([product[:, :rows_out, :], product[:, rows_out:, :]], axis=2)


def shift(x, axis, n, d):
    return lax.ppermute(x, axis, [(i, (i + d) % n) for i in range(n)])


def ring_gather(t):
    nz = lax.axis_size("cz")
    nx = lax.axis_size("cx")
    z = lax.axis_index("cz")
    x = lax.axis_index("cx")
    nb, comps, width, cols = t.shape
    other = shift(t, "cx", nx, 1)
    first = jnp.where(x == 0, t, other)
    second = jnp.where(x == 0, other, t)
    pair = jnp.stack([first, second], axis=2)
    buf = jnp.zeros((nb, comps, nz, nx, width, cols), t.dtype)
    buf = lax.dynamic_update_slice(buf, pair[:, :, None], (0, 0, z, 0, 0, 0))
    forward = nz // 2
    backward = nz - 1 - forward
    cur_f = pair
    cur_b = pair
    for k in range(1, forward + 1):
        if k == forward and nz % 2 == 0 and width % 2 == 0:
            half = width // 2
            a = shift(cur_f[:, :, :, :half], "cz", nz, 1)
            b = shift(cur_b[:, :, :, half:], "cz", nz, -1)
            piece = jnp.concatenate([a, b], axis=3)
            buf = lax.dynamic_update_slice(buf, piece[:, :, None], (0, 0, (z - k) % nz, 0, 0, 0))
            break
        cur_f = shift(cur_f, "cz", nz, 1)
        buf = lax.dynamic_update_slice(buf, cur_f[:, :, None], (0, 0, (z - k) % nz, 0, 0, 0))
        if k <= backward:
            cur_b = shift(cur_b, "cz", nz, -1)
            buf = lax.dynamic_update_slice(buf, cur_b[:, :, None], (0, 0, (z + k) % nz, 0, 0, 0))
    return buf.reshape(nb, comps, nz * nx * width, cols)


def shards(stem, branch):
    slab_count = stem.shape[2]
    order_size = stem.shape[3]
    row_count = lax.axis_size("row")
    share = order_size // row_count
    own_t = jnp.swapaxes(branch[0], -1, -2)
    first_t = ring_gather(own_t[:2])
    second_t = ring_gather(own_t[2:])

    block = stem[0, 0]
    half_first = right_piece(block, first_t[1]).astype(jnp.bfloat16)
    step_first = left_piece(half_first, first_t[0]).astype(jnp.bfloat16)
    outgoing = step_first.reshape(slab_count, row_count, share, 2, order_size)
    moved = lax.all_to_all(outgoing, "row", split_axis=1, concat_axis=1, tiled=True)
    items = moved.shape[0]
    flat = moved.reshape(items, order_size, 2, order_size)
    half_second = right_piece(flat, second_t[1]).astype(jnp.bfloat16)
    step_second = left_piece(half_second, second_t[0]).astype(jnp.bfloat16)
    leaving = step_second.reshape(slab_count, order_size, 2, row_count, share)
    arrived = lax.all_to_all(leaving, "row", split_axis=3, concat_axis=3, tiled=True)
    return arrived.reshape(1, 1, slab_count, order_size, 2, order_size)


def solution(mesh):
    n_col = mesh.shape["col"]
    split = Mesh(mesh.devices.reshape(mesh.shape["row"], n_col // 2, 2), ("row", "cz", "cx"))
    cols = ("cz", "cx")
    placed = (P("row", cols, None, None, None, None), P("row", None, None, None, cols))
    return jax.shard_map(
        shards,
        mesh=split,
        in_specs=placed,
        out_specs=P("row", cols, None, None, None, None),
        check_vma=False,
    )
```

```python
import jax
import jax.numpy as jnp
from jax import lax
from jax.sharding import Mesh
from jax.sharding import PartitionSpec as P


def right_piece(block, piece_t):
    items = block.shape[0]
    order_size = block.shape[1]
    flat = block.reshape(items * order_size, 2 * order_size)
    real_t = piece_t[0]
    imag_t = piece_t[1]
    weight = jnp.block([[real_t, imag_t], [-imag_t, real_t]])
    product = jnp.dot(flat, weight, preferred_element_type=jnp.float32)
    return product.reshape(items, order_size, 2, order_size)


def left_piece(block, piece_t):
    rows_out = piece_t.shape[2]
    real_in = block[:, :, 0, :]
    imag_in = block[:, :, 1, :]
    real_w = piece_t[0]
    imag_w = piece_t[1]
    weight_real = jnp.concatenate([real_w, imag_w], axis=1)
    weight_imag = jnp.concatenate([-imag_w, real_w], axis=1)
    product = jnp.einsum("ix,eij->exj", weight_real, real_in, preferred_element_type=jnp.float32)
    product = product + jnp.einsum(
        "ix,eij->exj", weight_imag, imag_in, preferred_element_type=jnp.float32
    )
    return jnp.stack([product[:, :rows_out, :], product[:, rows_out:, :]], axis=2)


def shift(x, axis, n, d):
    return lax.ppermute(x, axis, [(i, (i + d) % n) for i in range(n)])


def ring_gather(t):
    nz = lax.axis_size("cz")
    nx = lax.axis_size("cx")
    z = lax.axis_index("cz")
    x = lax.axis_index("cx")
    nb, comps, width, cols = t.shape
    other = shift(t, "cx", nx, 1)
    first = jnp.where(x == 0, t, other)
    second = jnp.where(x == 0, other, t)
    pair = jnp.stack([first, second], axis=2)
    buf = jnp.zeros((nb, comps, nz, nx, width, cols), t.dtype)
    buf = lax.dynamic_update_slice(buf, pair[:, :, None], (0, 0, z, 0, 0, 0))
    forward = nz // 2
    backward = nz - 1 - forward
    cur_f = pair
    cur_b = pair
    for k in range(1, forward + 1):
        if k == forward and nz % 2 == 0 and width % 2 == 0:
            half = width // 2
            a = shift(cur_f[:, :, :, :half], "cz", nz, 1)
            b = shift(cur_b[:, :, :, half:], "cz", nz, -1)
            piece = jnp.concatenate([a, b], axis=3)
            buf = lax.dynamic_update_slice(buf, piece[:, :, None], (0, 0, (z - k) % nz, 0, 0, 0))
            break
        cur_f = shift(cur_f, "cz", nz, 1)
        buf = lax.dynamic_update_slice(buf, cur_f[:, :, None], (0, 0, (z - k) % nz, 0, 0, 0))
        if k <= backward:
            cur_b = shift(cur_b, "cz", nz, -1)
            buf = lax.dynamic_update_slice(buf, cur_b[:, :, None], (0, 0, (z + k) % nz, 0, 0, 0))
    return buf.reshape(nb, comps, nz * nx * width, cols)


def shards(stem, branch):
    slab_count = stem.shape[2]
    order_size = stem.shape[3]
    row_count = lax.axis_size("row")
    share = order_size // row_count
    own_t = jnp.swapaxes(branch[0], -1, -2)
    first_t = ring_gather(own_t[:2])
    later, first_t = lax.optimization_barrier((own_t[2:], first_t))
    second_t = ring_gather(later)

    block = stem[0, 0]
    half_first = right_piece(block, first_t[1]).astype(jnp.bfloat16)
    step_first = left_piece(half_first, first_t[0]).astype(jnp.bfloat16)
    outgoing = step_first.reshape(slab_count, row_count, share, 2, order_size)
    moved = lax.all_to_all(outgoing, "row", split_axis=1, concat_axis=1, tiled=True)
    items = moved.shape[0]
    flat = moved.reshape(items, order_size, 2, order_size)
    half_second = right_piece(flat, second_t[1]).astype(jnp.bfloat16)
    step_second = left_piece(half_second, second_t[0]).astype(jnp.bfloat16)
    leaving = step_second.reshape(slab_count, order_size, 2, row_count, share)
    arrived = lax.all_to_all(leaving, "row", split_axis=3, concat_axis=3, tiled=True)
    return arrived.reshape(1, 1, slab_count, order_size, 2, order_size)


def solution(mesh):
    n_col = mesh.shape["col"]
    split = Mesh(mesh.devices.reshape(mesh.shape["row"], n_col // 2, 2), ("row", "cz", "cx"))
    cols = ("cz", "cx")
    placed = (P("row", cols, None, None, None, None), P("row", None, None, None, cols))
    return jax.shard_map(
        shards,
        mesh=split,
        in_specs=placed,
        out_specs=P("row", cols, None, None, None, None),
        check_vma=False,
    )
```

```python
import jax
import jax.numpy as jnp
from jax import lax
from jax.sharding import Mesh
from jax.sharding import PartitionSpec as P


def right_piece(block, piece_t):
    items = block.shape[0]
    order_size = block.shape[1]
    flat = block.reshape(items * order_size, 2 * order_size)
    real_t = piece_t[0]
    imag_t = piece_t[1]
    weight = jnp.block([[real_t, imag_t], [-imag_t, real_t]])
    product = jnp.dot(flat, weight, preferred_element_type=jnp.float32)
    return product.reshape(items, order_size, 2, order_size)


def left_piece(block, piece_t):
    rows_out = piece_t.shape[2]
    real_in = block[:, :, 0, :]
    imag_in = block[:, :, 1, :]
    real_w = piece_t[0]
    imag_w = piece_t[1]
    weight_real = jnp.concatenate([real_w, imag_w], axis=1)
    weight_imag = jnp.concatenate([-imag_w, real_w], axis=1)
    product = jnp.einsum("ix,eij->exj", weight_real, real_in, preferred_element_type=jnp.float32)
    product = product + jnp.einsum(
        "ix,eij->exj", weight_imag, imag_in, preferred_element_type=jnp.float32
    )
    return jnp.stack([product[:, :rows_out, :], product[:, rows_out:, :]], axis=2)


def shift(x, axis, n, d):
    return lax.ppermute(x, axis, [(i, (i + d) % n) for i in range(n)])


def ring_gather(t):
    nz = lax.axis_size("cz")
    nx = lax.axis_size("cx")
    z = lax.axis_index("cz")
    x = lax.axis_index("cx")
    nb, comps, width, cols = t.shape
    hw = width // 2
    other = shift(t, "cx", nx, 1)
    first = jnp.where(x == 0, t, other)
    second = jnp.where(x == 0, other, t)
    pair = jnp.stack([first, second], axis=2)
    buf = jnp.zeros((nb, comps, nz, nx, width, cols), t.dtype)
    buf = lax.dynamic_update_slice(buf, pair[:, :, None], (0, 0, z, 0, 0, 0))
    payload = jnp.concatenate(
        [pair[:, :, :, :hw].reshape(nb, comps, nx * hw, cols), t[:, :, hw:]], axis=2
    )

    def store(buf, piece, zs):
        shared = piece[:, :, : nx * hw].reshape(nb, comps, 1, nx, hw, cols)
        buf = lax.dynamic_update_slice(buf, shared, (0, 0, zs, 0, 0, 0))
        own = piece[:, :, nx * hw :].reshape(nb, comps, 1, 1, hw, cols)
        return lax.dynamic_update_slice(buf, own, (0, 0, zs, x, hw, 0))

    def store_other(buf, piece, zs):
        part = piece.reshape(nb, comps, 1, 1, hw, cols)
        return lax.dynamic_update_slice(buf, part, (0, 0, zs, 1 - x, hw, 0))

    forward = nz // 2
    rows = payload.shape[2]
    cur_f = payload
    cur_b = payload
    for k in range(1, forward + 1):
        if k == forward and nz % 2 == 0:
            a = shift(cur_f[:, :, : rows // 2], "cz", nz, 1)
            b = shift(cur_b[:, :, rows // 2 :], "cz", nz, -1)
            piece = jnp.concatenate([a, b], axis=2)
            zs = (z - k) % nz
            buf = store(buf, piece, zs)
            got = shift(piece[:, :, nx * hw :], "cx", nx, 1)
            buf = store_other(buf, got, zs)
            break
        cur_f = shift(cur_f, "cz", nz, 1)
        cur_b = shift(cur_b, "cz", nz, -1)
        buf = store(buf, cur_f, (z - k) % nz)
        buf = store(buf, cur_b, (z + k) % nz)
        sent = jnp.concatenate([cur_f[:, :, nx * hw :], cur_b[:, :, nx * hw :]], axis=2)
        got = shift(sent, "cx", nx, 1)
        buf = store_other(buf, got[:, :, :hw], (z - k) % nz)
        buf = store_other(buf, got[:, :, hw:], (z + k) % nz)
    return buf.reshape(nb, comps, nz * nx * width, cols)


def shards(stem, branch):
    slab_count = stem.shape[2]
    order_size = stem.shape[3]
    row_count = lax.axis_size("row")
    share = order_size // row_count
    own_t = jnp.swapaxes(branch[0], -1, -2)
    whole_t = ring_gather(own_t)
    first_t = whole_t[:2]
    second_t = whole_t[2:]

    block = stem[0, 0]
    half_first = right_piece(block, first_t[1]).astype(jnp.bfloat16)
    step_first = left_piece(half_first, first_t[0]).astype(jnp.bfloat16)
    outgoing = step_first.reshape(slab_count, row_count, share, 2, order_size)
    moved = lax.all_to_all(outgoing, "row", split_axis=1, concat_axis=1, tiled=True)
    items = moved.shape[0]
    flat = moved.reshape(items, order_size, 2, order_size)
    half_second = right_piece(flat, second_t[1]).astype(jnp.bfloat16)
    step_second = left_piece(half_second, second_t[0]).astype(jnp.bfloat16)
    leaving = step_second.reshape(slab_count, order_size, 2, row_count, share)
    arrived = lax.all_to_all(leaving, "row", split_axis=3, concat_axis=3, tiled=True)
    return arrived.reshape(1, 1, slab_count, order_size, 2, order_size)


def solution(mesh):
    n_col = mesh.shape["col"]
    split = Mesh(mesh.devices.reshape(mesh.shape["row"], n_col // 2, 2), ("row", "cz", "cx"))
    cols = ("cz", "cx")
    placed = (P("row", cols, None, None, None, None), P("row", None, None, None, cols))
    return jax.shard_map(
        shards,
        mesh=split,
        in_specs=placed,
        out_specs=P("row", cols, None, None, None, None),
        check_vma=False,
    )
```

```python
import jax
import jax.numpy as jnp
from jax import lax
from jax.sharding import Mesh
from jax.sharding import PartitionSpec as P


def right_piece(block, piece_t):
    items = block.shape[0]
    order_size = block.shape[1]
    flat = block.reshape(items * order_size, 2 * order_size)
    real_t = piece_t[0]
    imag_t = piece_t[1]
    weight = jnp.block([[real_t, imag_t], [-imag_t, real_t]])
    product = jnp.dot(flat, weight, preferred_element_type=jnp.float32)
    return product.reshape(items, order_size, 2, order_size)


def right_planar(planar, piece_t):
    real_t = piece_t[0]
    imag_t = piece_t[1]
    top = jnp.concatenate([real_t, imag_t], axis=1)
    bottom = jnp.concatenate([-imag_t, real_t], axis=1)
    product = jnp.dot(planar[0], top, preferred_element_type=jnp.float32)
    product = product + jnp.dot(planar[1], bottom, preferred_element_type=jnp.float32)
    return product.reshape(planar.shape[1], 2, piece_t.shape[2])


def left_planar(block, piece_t):
    real_w = piece_t[0]
    imag_w = piece_t[1]
    weight_real = jnp.concatenate([real_w, imag_w], axis=1)
    weight_imag = jnp.concatenate([-imag_w, real_w], axis=1)
    product = jnp.einsum("ix,ij->xj", weight_real, block[:, 0, :], preferred_element_type=jnp.float32)
    product = product + jnp.einsum(
        "ix,ij->xj", weight_imag, block[:, 1, :], preferred_element_type=jnp.float32
    )
    return product.reshape(2, piece_t.shape[2], block.shape[2])


def left_piece(block, piece_t):
    rows_out = piece_t.shape[2]
    real_in = block[:, :, 0, :]
    imag_in = block[:, :, 1, :]
    real_w = piece_t[0]
    imag_w = piece_t[1]
    weight_real = jnp.concatenate([real_w, imag_w], axis=1)
    weight_imag = jnp.concatenate([-imag_w, real_w], axis=1)
    product = jnp.einsum("ix,eij->exj", weight_real, real_in, preferred_element_type=jnp.float32)
    product = product + jnp.einsum(
        "ix,eij->exj", weight_imag, imag_in, preferred_element_type=jnp.float32
    )
    return jnp.stack([product[:, :rows_out, :], product[:, rows_out:, :]], axis=2)


def shift(x, axis, n, d):
    return lax.ppermute(x, axis, [(i, (i + d) % n) for i in range(n)])


def ring_gather(t):
    nz = lax.axis_size("cz")
    nx = lax.axis_size("cx")
    z = lax.axis_index("cz")
    x = lax.axis_index("cx")
    nb, comps, width, cols = t.shape
    other = shift(t, "cx", nx, 1)
    first = jnp.where(x == 0, t, other)
    second = jnp.where(x == 0, other, t)
    pair = jnp.stack([first, second], axis=2)
    buf = jnp.zeros((nb, comps, nz, nx, width, cols), t.dtype)
    buf = lax.dynamic_update_slice(buf, pair[:, :, None], (0, 0, z, 0, 0, 0))
    forward = nz // 2
    backward = nz - 1 - forward
    cur_f = pair
    cur_b = pair
    for k in range(1, forward + 1):
        if k == forward and nz % 2 == 0 and width % 2 == 0:
            half = width // 2
            a = shift(cur_f[:, :, :, :half], "cz", nz, 1)
            b = shift(cur_b[:, :, :, half:], "cz", nz, -1)
            piece = jnp.concatenate([a, b], axis=3)
            buf = lax.dynamic_update_slice(buf, piece[:, :, None], (0, 0, (z - k) % nz, 0, 0, 0))
            break
        cur_f = shift(cur_f, "cz", nz, 1)
        buf = lax.dynamic_update_slice(buf, cur_f[:, :, None], (0, 0, (z - k) % nz, 0, 0, 0))
        if k <= backward:
            cur_b = shift(cur_b, "cz", nz, -1)
            buf = lax.dynamic_update_slice(buf, cur_b[:, :, None], (0, 0, (z + k) % nz, 0, 0, 0))
    return buf.reshape(nb, comps, nz * nx * width, cols)


def shards(stem, branch):
    slab_count = stem.shape[2]
    order_size = stem.shape[3]
    row_count = lax.axis_size("row")
    share = order_size // row_count
    own_t = jnp.swapaxes(branch[0], -1, -2)
    first_t = ring_gather(own_t[:2])
    second_t = ring_gather(own_t[2:])

    block = stem[0, 0]
    half_first = right_piece(block, first_t[1]).astype(jnp.bfloat16)
    step_first = left_planar(half_first[0], first_t[0]).astype(jnp.bfloat16)
    outgoing = step_first.reshape(2, row_count, share, order_size)
    moved = lax.all_to_all(outgoing, "row", split_axis=1, concat_axis=1, tiled=True)
    planar = moved.reshape(2, order_size, order_size)
    half_second = right_planar(planar, second_t[1]).astype(jnp.bfloat16)[None]
    step_second = left_piece(half_second, second_t[0]).astype(jnp.bfloat16)
    leaving = step_second.reshape(slab_count, order_size, 2, row_count, share)
    arrived = lax.all_to_all(leaving, "row", split_axis=3, concat_axis=3, tiled=True)
    return arrived.reshape(1, 1, slab_count, order_size, 2, order_size)


def solution(mesh):
    n_col = mesh.shape["col"]
    split = Mesh(mesh.devices.reshape(mesh.shape["row"], n_col // 2, 2), ("row", "cz", "cx"))
    cols = ("cz", "cx")
    placed = (P("row", cols, None, None, None, None), P("row", None, None, None, cols))
    return jax.shard_map(
        shards,
        mesh=split,
        in_specs=placed,
        out_specs=P("row", cols, None, None, None, None),
        check_vma=False,
    )
```

```python
import jax
import jax.numpy as jnp
from jax import lax
from jax.sharding import Mesh
from jax.sharding import PartitionSpec as P


def right_piece(block, piece_t):
    items = block.shape[0]
    order_size = block.shape[1]
    flat = block.reshape(items * order_size, 2 * order_size)
    real_t = piece_t[0]
    imag_t = piece_t[1]
    weight = jnp.block([[real_t, imag_t], [-imag_t, real_t]])
    product = jnp.dot(flat, weight, preferred_element_type=jnp.float32)
    return product.reshape(items, order_size, 2, order_size)


def right_planar(planar, piece_t):
    real_t = piece_t[0]
    imag_t = piece_t[1]
    top = jnp.concatenate([real_t, imag_t], axis=1)
    bottom = jnp.concatenate([-imag_t, real_t], axis=1)
    product = jnp.dot(planar[0], top, preferred_element_type=jnp.float32)
    product = product + jnp.dot(planar[1], bottom, preferred_element_type=jnp.float32)
    cols = piece_t.shape[2]
    return product[:, :cols], product[:, cols:]


def left_planar(block, piece_t):
    real_w = piece_t[0]
    imag_w = piece_t[1]
    weight_real = jnp.concatenate([real_w, imag_w], axis=1)
    weight_imag = jnp.concatenate([-imag_w, real_w], axis=1)
    product = jnp.einsum("ix,ij->xj", weight_real, block[:, 0, :], preferred_element_type=jnp.float32)
    product = product + jnp.einsum(
        "ix,ij->xj", weight_imag, block[:, 1, :], preferred_element_type=jnp.float32
    )
    return product.reshape(2, piece_t.shape[2], block.shape[2])


def left_halves(real_in, imag_in, piece_t):
    rows_out = piece_t.shape[2]
    real_w = piece_t[0]
    imag_w = piece_t[1]
    weight_real = jnp.concatenate([real_w, imag_w], axis=1)
    weight_imag = jnp.concatenate([-imag_w, real_w], axis=1)
    product = jnp.einsum("ix,ij->xj", weight_real, real_in, preferred_element_type=jnp.float32)
    product = product + jnp.einsum(
        "ix,ij->xj", weight_imag, imag_in, preferred_element_type=jnp.float32
    )
    return jnp.stack([product[:rows_out], product[rows_out:]], axis=1)


def left_piece(block, piece_t):
    rows_out = piece_t.shape[2]
    real_in = block[:, :, 0, :]
    imag_in = block[:, :, 1, :]
    real_w = piece_t[0]
    imag_w = piece_t[1]
    weight_real = jnp.concatenate([real_w, imag_w], axis=1)
    weight_imag = jnp.concatenate([-imag_w, real_w], axis=1)
    product = jnp.einsum("ix,eij->exj", weight_real, real_in, preferred_element_type=jnp.float32)
    product = product + jnp.einsum(
        "ix,eij->exj", weight_imag, imag_in, preferred_element_type=jnp.float32
    )
    return jnp.stack([product[:, :rows_out, :], product[:, rows_out:, :]], axis=2)


def shift(x, axis, n, d):
    return lax.ppermute(x, axis, [(i, (i + d) % n) for i in range(n)])


def ring_gather(t):
    nz = lax.axis_size("cz")
    nx = lax.axis_size("cx")
    z = lax.axis_index("cz")
    x = lax.axis_index("cx")
    nb, comps, width, cols = t.shape
    other = shift(t, "cx", nx, 1)
    first = jnp.where(x == 0, t, other)
    second = jnp.where(x == 0, other, t)
    pair = jnp.stack([first, second], axis=2)
    buf = jnp.zeros((nb, comps, nz, nx, width, cols), t.dtype)
    buf = lax.dynamic_update_slice(buf, pair[:, :, None], (0, 0, z, 0, 0, 0))
    forward = nz // 2
    backward = nz - 1 - forward
    cur_f = pair
    cur_b = pair
    for k in range(1, forward + 1):
        if k == forward and nz % 2 == 0 and width % 2 == 0:
            half = width // 2
            a = shift(cur_f[:, :, :, :half], "cz", nz, 1)
            b = shift(cur_b[:, :, :, half:], "cz", nz, -1)
            piece = jnp.concatenate([a, b], axis=3)
            buf = lax.dynamic_update_slice(buf, piece[:, :, None], (0, 0, (z - k) % nz, 0, 0, 0))
            break
        cur_f = shift(cur_f, "cz", nz, 1)
        buf = lax.dynamic_update_slice(buf, cur_f[:, :, None], (0, 0, (z - k) % nz, 0, 0, 0))
        if k <= backward:
            cur_b = shift(cur_b, "cz", nz, -1)
            buf = lax.dynamic_update_slice(buf, cur_b[:, :, None], (0, 0, (z + k) % nz, 0, 0, 0))
    return buf.reshape(nb, comps, nz * nx * width, cols)


def shards(stem, branch):
    slab_count = stem.shape[2]
    order_size = stem.shape[3]
    row_count = lax.axis_size("row")
    share = order_size // row_count
    own_t = jnp.swapaxes(branch[0], -1, -2)
    first_t = ring_gather(own_t[:2])
    second_t = ring_gather(own_t[2:])

    block = stem[0, 0]
    half_first = right_piece(block, first_t[1]).astype(jnp.bfloat16)
    step_first = left_planar(half_first[0], first_t[0]).astype(jnp.bfloat16)
    outgoing = step_first.reshape(2, row_count, share, order_size)
    moved = lax.all_to_all(outgoing, "row", split_axis=1, concat_axis=1, tiled=True)
    planar = moved.reshape(2, order_size, order_size)
    real_half, imag_half = right_planar(planar, second_t[1])
    step_second = left_halves(
        real_half.astype(jnp.bfloat16), imag_half.astype(jnp.bfloat16), second_t[0]
    ).astype(jnp.bfloat16)
    leaving = step_second.reshape(slab_count, order_size, 2, row_count, share)
    arrived = lax.all_to_all(leaving, "row", split_axis=3, concat_axis=3, tiled=True)
    return arrived.reshape(1, 1, slab_count, order_size, 2, order_size)


def solution(mesh):
    n_col = mesh.shape["col"]
    split = Mesh(mesh.devices.reshape(mesh.shape["row"], n_col // 2, 2), ("row", "cz", "cx"))
    cols = ("cz", "cx")
    placed = (P("row", cols, None, None, None, None), P("row", None, None, None, cols))
    return jax.shard_map(
        shards,
        mesh=split,
        in_specs=placed,
        out_specs=P("row", cols, None, None, None, None),
        check_vma=False,
    )
```

```python
import jax
import jax.numpy as jnp
from jax import lax
from jax.sharding import Mesh
from jax.sharding import PartitionSpec as P


def right_piece(block, piece_t):
    items = block.shape[0]
    order_size = block.shape[1]
    flat = block.reshape(items * order_size, 2 * order_size)
    real_t = piece_t[0]
    imag_t = piece_t[1]
    weight = jnp.block([[real_t, imag_t], [-imag_t, real_t]])
    product = jnp.dot(flat, weight, preferred_element_type=jnp.float32)
    return product.reshape(items, order_size, 2, order_size)


def right_blocks(grouped, piece_t):
    real_t = piece_t[0]
    imag_t = piece_t[1]
    top = jnp.concatenate([real_t, imag_t], axis=1)
    bottom = jnp.concatenate([-imag_t, real_t], axis=1)
    weight = jnp.stack([top, bottom], axis=0)
    product = jnp.einsum("pcly,cyk->plk", grouped, weight, preferred_element_type=jnp.float32)
    cols = piece_t.shape[2]
    product = product.reshape(-1, 2 * cols)
    return product[:, :cols], product[:, cols:]


def left_blocks(block, piece_t, parts):
    rows_in = piece_t.shape[1]
    real_w = piece_t[0].reshape(rows_in, parts, 1, -1)
    imag_w = piece_t[1].reshape(rows_in, parts, 1, -1)
    weight_real = jnp.concatenate([real_w, imag_w], axis=2).reshape(rows_in, -1)
    weight_imag = jnp.concatenate([-imag_w, real_w], axis=2).reshape(rows_in, -1)
    product = jnp.einsum("ix,ij->xj", weight_real, block[:, 0, :], preferred_element_type=jnp.float32)
    product = product + jnp.einsum(
        "ix,ij->xj", weight_imag, block[:, 1, :], preferred_element_type=jnp.float32
    )
    return product.reshape(parts, 2, -1, block.shape[2])


def left_halves(real_in, imag_in, piece_t):
    rows_out = piece_t.shape[2]
    real_w = piece_t[0]
    imag_w = piece_t[1]
    weight_real = jnp.concatenate([real_w, imag_w], axis=1)
    weight_imag = jnp.concatenate([-imag_w, real_w], axis=1)
    product = jnp.einsum("ix,ij->xj", weight_real, real_in, preferred_element_type=jnp.float32)
    product = product + jnp.einsum(
        "ix,ij->xj", weight_imag, imag_in, preferred_element_type=jnp.float32
    )
    return jnp.stack([product[:rows_out], product[rows_out:]], axis=1)


def left_piece(block, piece_t):
    rows_out = piece_t.shape[2]
    real_in = block[:, :, 0, :]
    imag_in = block[:, :, 1, :]
    real_w = piece_t[0]
    imag_w = piece_t[1]
    weight_real = jnp.concatenate([real_w, imag_w], axis=1)
    weight_imag = jnp.concatenate([-imag_w, real_w], axis=1)
    product = jnp.einsum("ix,eij->exj", weight_real, real_in, preferred_element_type=jnp.float32)
    product = product + jnp.einsum(
        "ix,eij->exj", weight_imag, imag_in, preferred_element_type=jnp.float32
    )
    return jnp.stack([product[:, :rows_out, :], product[:, rows_out:, :]], axis=2)


def shift(x, axis, n, d):
    return lax.ppermute(x, axis, [(i, (i + d) % n) for i in range(n)])


def ring_gather(t):
    nz = lax.axis_size("cz")
    nx = lax.axis_size("cx")
    z = lax.axis_index("cz")
    x = lax.axis_index("cx")
    nb, comps, width, cols = t.shape
    other = shift(t, "cx", nx, 1)
    first = jnp.where(x == 0, t, other)
    second = jnp.where(x == 0, other, t)
    pair = jnp.stack([first, second], axis=2)
    buf = jnp.zeros((nb, comps, nz, nx, width, cols), t.dtype)
    buf = lax.dynamic_update_slice(buf, pair[:, :, None], (0, 0, z, 0, 0, 0))
    forward = nz // 2
    backward = nz - 1 - forward
    cur_f = pair
    cur_b = pair
    for k in range(1, forward + 1):
        if k == forward and nz % 2 == 0 and width % 2 == 0:
            half = width // 2
            a = shift(cur_f[:, :, :, :half], "cz", nz, 1)
            b = shift(cur_b[:, :, :, half:], "cz", nz, -1)
            piece = jnp.concatenate([a, b], axis=3)
            buf = lax.dynamic_update_slice(buf, piece[:, :, None], (0, 0, (z - k) % nz, 0, 0, 0))
            break
        cur_f = shift(cur_f, "cz", nz, 1)
        buf = lax.dynamic_update_slice(buf, cur_f[:, :, None], (0, 0, (z - k) % nz, 0, 0, 0))
        if k <= backward:
            cur_b = shift(cur_b, "cz", nz, -1)
            buf = lax.dynamic_update_slice(buf, cur_b[:, :, None], (0, 0, (z + k) % nz, 0, 0, 0))
    return buf.reshape(nb, comps, nz * nx * width, cols)


def shards(stem, branch):
    slab_count = stem.shape[2]
    order_size = stem.shape[3]
    row_count = lax.axis_size("row")
    share = order_size // row_count
    own_t = jnp.swapaxes(branch[0], -1, -2)
    first_t = ring_gather(own_t[:2])
    second_t = ring_gather(own_t[2:])

    block = stem[0, 0]
    half_first = right_piece(block, first_t[1]).astype(jnp.bfloat16)
    outgoing = left_blocks(half_first[0], first_t[0], row_count).astype(jnp.bfloat16)
    moved = lax.all_to_all(outgoing, "row", split_axis=0, concat_axis=0, tiled=True)
    real_half, imag_half = right_blocks(moved, second_t[1])
    step_second = left_halves(
        real_half.astype(jnp.bfloat16), imag_half.astype(jnp.bfloat16), second_t[0]
    ).astype(jnp.bfloat16)
    leaving = step_second.reshape(slab_count, order_size, 2, row_count, share)
    arrived = lax.all_to_all(leaving, "row", split_axis=3, concat_axis=3, tiled=True)
    return arrived.reshape(1, 1, slab_count, order_size, 2, order_size)


def solution(mesh):
    n_col = mesh.shape["col"]
    split = Mesh(mesh.devices.reshape(mesh.shape["row"], n_col // 2, 2), ("row", "cz", "cx"))
    cols = ("cz", "cx")
    placed = (P("row", cols, None, None, None, None), P("row", None, None, None, cols))
    return jax.shard_map(
        shards,
        mesh=split,
        in_specs=placed,
        out_specs=P("row", cols, None, None, None, None),
        check_vma=False,
    )
```

```python
import jax
import jax.numpy as jnp
from jax import lax
from jax.sharding import Mesh
from jax.sharding import PartitionSpec as P


def right_piece(block, piece_t):
    items = block.shape[0]
    order_size = block.shape[1]
    flat = block.reshape(items * order_size, 2 * order_size)
    real_t = piece_t[0]
    imag_t = piece_t[1]
    weight = jnp.block([[real_t, imag_t], [-imag_t, real_t]])
    product = jnp.dot(flat, weight, preferred_element_type=jnp.float32)
    return product.reshape(items, order_size, 2, order_size)


def right_planar(planar, piece_t):
    real_t = piece_t[0]
    imag_t = piece_t[1]
    top = jnp.concatenate([real_t, imag_t], axis=1)
    bottom = jnp.concatenate([-imag_t, real_t], axis=1)
    product = jnp.dot(planar[0], top, preferred_element_type=jnp.float32)
    product = product + jnp.dot(planar[1], bottom, preferred_element_type=jnp.float32)
    cols = piece_t.shape[2]
    return product[:, :cols], product[:, cols:]


def left_planar(block, piece_t):
    real_w = piece_t[0]
    imag_w = piece_t[1]
    weight_real = jnp.concatenate([real_w, imag_w], axis=1)
    weight_imag = jnp.concatenate([-imag_w, real_w], axis=1)
    product = jnp.einsum("ix,ij->xj", weight_real, block[:, 0, :], preferred_element_type=jnp.float32)
    product = product + jnp.einsum(
        "ix,ij->xj", weight_imag, block[:, 1, :], preferred_element_type=jnp.float32
    )
    return product.reshape(2, piece_t.shape[2], block.shape[2])


def left_halves(real_in, imag_in, piece_t):
    rows_out = piece_t.shape[2]
    real_w = piece_t[0]
    imag_w = piece_t[1]
    weight_real = jnp.concatenate([real_w, imag_w], axis=1)
    weight_imag = jnp.concatenate([-imag_w, real_w], axis=1)
    product = jnp.einsum("ix,ij->xj", weight_real, real_in, preferred_element_type=jnp.float32)
    product = product + jnp.einsum(
        "ix,ij->xj", weight_imag, imag_in, preferred_element_type=jnp.float32
    )
    return jnp.stack([product[:rows_out], product[rows_out:]], axis=1)


def left_piece(block, piece_t):
    rows_out = piece_t.shape[2]
    real_in = block[:, :, 0, :]
    imag_in = block[:, :, 1, :]
    real_w = piece_t[0]
    imag_w = piece_t[1]
    weight_real = jnp.concatenate([real_w, imag_w], axis=1)
    weight_imag = jnp.concatenate([-imag_w, real_w], axis=1)
    product = jnp.einsum("ix,eij->exj", weight_real, real_in, preferred_element_type=jnp.float32)
    product = product + jnp.einsum(
        "ix,eij->exj", weight_imag, imag_in, preferred_element_type=jnp.float32
    )
    return jnp.stack([product[:, :rows_out, :], product[:, rows_out:, :]], axis=2)


def shift(x, axis, n, d):
    return lax.ppermute(x, axis, [(i, (i + d) % n) for i in range(n)])


def ring_gather(t, other):
    nz = lax.axis_size("cz")
    nx = lax.axis_size("cx")
    z = lax.axis_index("cz")
    x = lax.axis_index("cx")
    nb, comps, width, cols = t.shape
    first = jnp.where(x == 0, t, other)
    second = jnp.where(x == 0, other, t)
    pair = jnp.stack([first, second], axis=2)
    buf = jnp.zeros((nb, comps, nz, nx, width, cols), t.dtype)
    buf = lax.dynamic_update_slice(buf, pair[:, :, None], (0, 0, z, 0, 0, 0))
    forward = nz // 2
    backward = nz - 1 - forward
    cur_f = pair
    cur_b = pair
    for k in range(1, forward + 1):
        if k == forward and nz % 2 == 0 and width % 2 == 0:
            half = width // 2
            a = shift(cur_f[:, :, :, :half], "cz", nz, 1)
            b = shift(cur_b[:, :, :, half:], "cz", nz, -1)
            piece = jnp.concatenate([a, b], axis=3)
            buf = lax.dynamic_update_slice(buf, piece[:, :, None], (0, 0, (z - k) % nz, 0, 0, 0))
            break
        cur_f = shift(cur_f, "cz", nz, 1)
        buf = lax.dynamic_update_slice(buf, cur_f[:, :, None], (0, 0, (z - k) % nz, 0, 0, 0))
        if k <= backward:
            cur_b = shift(cur_b, "cz", nz, -1)
            buf = lax.dynamic_update_slice(buf, cur_b[:, :, None], (0, 0, (z + k) % nz, 0, 0, 0))
    return buf.reshape(nb, comps, nz * nx * width, cols)


def shards(stem, branch):
    slab_count = stem.shape[2]
    order_size = stem.shape[3]
    row_count = lax.axis_size("row")
    share = order_size // row_count
    own_t = jnp.swapaxes(branch[0], -1, -2)
    partner_t = shift(own_t, "cx", lax.axis_size("cx"), 1)
    first_t = ring_gather(own_t[:2], partner_t[:2])
    second_t = ring_gather(own_t[2:], partner_t[2:])

    block = stem[0, 0]
    half_first = right_piece(block, first_t[1]).astype(jnp.bfloat16)
    step_first = left_planar(half_first[0], first_t[0]).astype(jnp.bfloat16)
    outgoing = step_first.reshape(2, row_count, share, order_size)
    moved = lax.all_to_all(outgoing, "row", split_axis=1, concat_axis=1, tiled=True)
    planar = moved.reshape(2, order_size, order_size)
    real_half, imag_half = right_planar(planar, second_t[1])
    step_second = left_halves(
        real_half.astype(jnp.bfloat16), imag_half.astype(jnp.bfloat16), second_t[0]
    ).astype(jnp.bfloat16)
    leaving = step_second.reshape(slab_count, order_size, 2, row_count, share)
    arrived = lax.all_to_all(leaving, "row", split_axis=3, concat_axis=3, tiled=True)
    return arrived.reshape(1, 1, slab_count, order_size, 2, order_size)


def solution(mesh):
    n_col = mesh.shape["col"]
    split = Mesh(mesh.devices.reshape(mesh.shape["row"], n_col // 2, 2), ("row", "cz", "cx"))
    cols = ("cz", "cx")
    placed = (P("row", cols, None, None, None, None), P("row", None, None, None, cols))
    return jax.shard_map(
        shards,
        mesh=split,
        in_specs=placed,
        out_specs=P("row", cols, None, None, None, None),
        check_vma=False,
    )
```

```python
import jax
import jax.numpy as jnp
from jax import lax
from jax.sharding import Mesh
from jax.sharding import PartitionSpec as P


def right_piece(block, piece_t):
    items = block.shape[0]
    order_size = block.shape[1]
    flat = block.reshape(items * order_size, 2 * order_size)
    real_t = piece_t[0]
    imag_t = piece_t[1]
    weight = jnp.block([[real_t, imag_t], [-imag_t, real_t]])
    product = jnp.dot(flat, weight, preferred_element_type=jnp.float32)
    return product.reshape(items, order_size, 2, order_size)


def right_planar(planar, piece_t):
    real_t = piece_t[0]
    imag_t = piece_t[1]
    top = jnp.concatenate([real_t, imag_t], axis=1)
    bottom = jnp.concatenate([-imag_t, real_t], axis=1)
    product = jnp.dot(planar[0], top, preferred_element_type=jnp.float32)
    product = product + jnp.dot(planar[1], bottom, preferred_element_type=jnp.float32)
    cols = piece_t.shape[2]
    return product[:, :cols], product[:, cols:]


def left_planar(block, piece_t):
    real_w = piece_t[0]
    imag_w = piece_t[1]
    weight_real = jnp.concatenate([real_w, imag_w], axis=1)
    weight_imag = jnp.concatenate([-imag_w, real_w], axis=1)
    product = jnp.einsum("ix,ij->xj", weight_real, block[:, 0, :], preferred_element_type=jnp.float32)
    product = product + jnp.einsum(
        "ix,ij->xj", weight_imag, block[:, 1, :], preferred_element_type=jnp.float32
    )
    return product.reshape(2, piece_t.shape[2], block.shape[2])


def left_halves(real_in, imag_in, piece_t):
    rows_out = piece_t.shape[2]
    real_w = piece_t[0]
    imag_w = piece_t[1]
    weight_real = jnp.concatenate([real_w, imag_w], axis=1)
    weight_imag = jnp.concatenate([-imag_w, real_w], axis=1)
    product = jnp.einsum("ix,ij->xj", weight_real, real_in, preferred_element_type=jnp.float32)
    product = product + jnp.einsum(
        "ix,ij->xj", weight_imag, imag_in, preferred_element_type=jnp.float32
    )
    return jnp.stack([product[:rows_out], product[rows_out:]], axis=1)


def left_piece(block, piece_t):
    rows_out = piece_t.shape[2]
    real_in = block[:, :, 0, :]
    imag_in = block[:, :, 1, :]
    real_w = piece_t[0]
    imag_w = piece_t[1]
    weight_real = jnp.concatenate([real_w, imag_w], axis=1)
    weight_imag = jnp.concatenate([-imag_w, real_w], axis=1)
    product = jnp.einsum("ix,eij->exj", weight_real, real_in, preferred_element_type=jnp.float32)
    product = product + jnp.einsum(
        "ix,eij->exj", weight_imag, imag_in, preferred_element_type=jnp.float32
    )
    return jnp.stack([product[:, :rows_out, :], product[:, rows_out:, :]], axis=2)


def shift(x, axis, n, d):
    return lax.ppermute(x, axis, [(i, (i + d) % n) for i in range(n)])


def ring_gather(t, hold=None):
    nz = lax.axis_size("cz")
    nx = lax.axis_size("cx")
    z = lax.axis_index("cz")
    x = lax.axis_index("cx")
    nb, comps, width, cols = t.shape
    other = shift(t, "cx", nx, 1)
    first = jnp.where(x == 0, t, other)
    second = jnp.where(x == 0, other, t)
    pair = jnp.stack([first, second], axis=2)
    buf = jnp.zeros((nb, comps, nz, nx, width, cols), t.dtype)
    buf = lax.dynamic_update_slice(buf, pair[:, :, None], (0, 0, z, 0, 0, 0))
    forward = nz // 2
    backward = nz - 1 - forward
    cur_f = pair
    cur_b = pair
    for k in range(1, forward + 1):
        if k == forward and nz % 2 == 0 and width % 2 == 0:
            half = width // 2
            if hold is not None:
                (cur_f, cur_b), hold = lax.optimization_barrier(((cur_f, cur_b), hold))
            a = shift(cur_f[:, :, :, :half], "cz", nz, 1)
            b = shift(cur_b[:, :, :, half:], "cz", nz, -1)
            piece = jnp.concatenate([a, b], axis=3)
            buf = lax.dynamic_update_slice(buf, piece[:, :, None], (0, 0, (z - k) % nz, 0, 0, 0))
            break
        cur_f = shift(cur_f, "cz", nz, 1)
        buf = lax.dynamic_update_slice(buf, cur_f[:, :, None], (0, 0, (z - k) % nz, 0, 0, 0))
        if k <= backward:
            cur_b = shift(cur_b, "cz", nz, -1)
            buf = lax.dynamic_update_slice(buf, cur_b[:, :, None], (0, 0, (z + k) % nz, 0, 0, 0))
    return buf.reshape(nb, comps, nz * nx * width, cols), hold


def shards(stem, branch):
    slab_count = stem.shape[2]
    order_size = stem.shape[3]
    row_count = lax.axis_size("row")
    share = order_size // row_count
    own_t = jnp.swapaxes(branch[0], -1, -2)
    first_t, _ = ring_gather(own_t[:2])

    block = stem[0, 0]
    half_first = right_piece(block, first_t[1]).astype(jnp.bfloat16)
    step_first = left_planar(half_first[0], first_t[0]).astype(jnp.bfloat16)
    second_t, step_first = ring_gather(own_t[2:], hold=step_first)
    outgoing = step_first.reshape(2, row_count, share, order_size)
    moved = lax.all_to_all(outgoing, "row", split_axis=1, concat_axis=1, tiled=True)
    planar = moved.reshape(2, order_size, order_size)
    real_half, imag_half = right_planar(planar, second_t[1])
    step_second = left_halves(
        real_half.astype(jnp.bfloat16), imag_half.astype(jnp.bfloat16), second_t[0]
    ).astype(jnp.bfloat16)
    leaving = step_second.reshape(slab_count, order_size, 2, row_count, share)
    arrived = lax.all_to_all(leaving, "row", split_axis=3, concat_axis=3, tiled=True)
    return arrived.reshape(1, 1, slab_count, order_size, 2, order_size)


def solution(mesh):
    n_col = mesh.shape["col"]
    split = Mesh(mesh.devices.reshape(mesh.shape["row"], n_col // 2, 2), ("row", "cz", "cx"))
    cols = ("cz", "cx")
    placed = (P("row", cols, None, None, None, None), P("row", None, None, None, cols))
    return jax.shard_map(
        shards,
        mesh=split,
        in_specs=placed,
        out_specs=P("row", cols, None, None, None, None),
        check_vma=False,
    )
```

```python
import jax
import jax.numpy as jnp
from jax import lax
from jax.sharding import Mesh
from jax.sharding import PartitionSpec as P


def right_piece(block, piece_t):
    items = block.shape[0]
    order_size = block.shape[1]
    flat = block.reshape(items * order_size, 2 * order_size)
    real_t = piece_t[0]
    imag_t = piece_t[1]
    weight = jnp.block([[real_t, imag_t], [-imag_t, real_t]])
    product = jnp.dot(flat, weight, preferred_element_type=jnp.float32)
    return product.reshape(items, order_size, 2, order_size)


def right_planar(planar, piece_t):
    real_t = piece_t[0]
    imag_t = piece_t[1]
    top = jnp.concatenate([real_t, imag_t], axis=1)
    bottom = jnp.concatenate([-imag_t, real_t], axis=1)
    product = jnp.dot(planar[0], top, preferred_element_type=jnp.float32)
    product = product + jnp.dot(planar[1], bottom, preferred_element_type=jnp.float32)
    cols = piece_t.shape[2]
    return product[:, :cols], product[:, cols:]


def left_planar(block, piece_t):
    real_w = piece_t[0]
    imag_w = piece_t[1]
    weight_real = jnp.concatenate([real_w, imag_w], axis=1)
    weight_imag = jnp.concatenate([-imag_w, real_w], axis=1)
    product = jnp.einsum("ix,ij->xj", weight_real, block[:, 0, :], preferred_element_type=jnp.float32)
    product = product + jnp.einsum(
        "ix,ij->xj", weight_imag, block[:, 1, :], preferred_element_type=jnp.float32
    )
    return product.reshape(2, piece_t.shape[2], block.shape[2])


def left_halves(real_in, imag_in, piece_t):
    rows_out = piece_t.shape[2]
    real_w = piece_t[0]
    imag_w = piece_t[1]
    weight_real = jnp.concatenate([real_w, imag_w], axis=1)
    weight_imag = jnp.concatenate([-imag_w, real_w], axis=1)
    product = jnp.einsum("ix,ij->xj", weight_real, real_in, preferred_element_type=jnp.float32)
    product = product + jnp.einsum(
        "ix,ij->xj", weight_imag, imag_in, preferred_element_type=jnp.float32
    )
    return jnp.stack([product[:rows_out], product[rows_out:]], axis=1)


def left_piece(block, piece_t):
    rows_out = piece_t.shape[2]
    real_in = block[:, :, 0, :]
    imag_in = block[:, :, 1, :]
    real_w = piece_t[0]
    imag_w = piece_t[1]
    weight_real = jnp.concatenate([real_w, imag_w], axis=1)
    weight_imag = jnp.concatenate([-imag_w, real_w], axis=1)
    product = jnp.einsum("ix,eij->exj", weight_real, real_in, preferred_element_type=jnp.float32)
    product = product + jnp.einsum(
        "ix,eij->exj", weight_imag, imag_in, preferred_element_type=jnp.float32
    )
    return jnp.stack([product[:, :rows_out, :], product[:, rows_out:, :]], axis=2)


def shift(x, axis, n, d):
    return lax.ppermute(x, axis, [(i, (i + d) % n) for i in range(n)])


def ring_gather(t, hold=None):
    nz = lax.axis_size("cz")
    nx = lax.axis_size("cx")
    z = lax.axis_index("cz")
    x = lax.axis_index("cx")
    nb, comps, width, cols = t.shape
    other = shift(t, "cx", nx, 1)
    first = jnp.where(x == 0, t, other)
    second = jnp.where(x == 0, other, t)
    pair = jnp.stack([first, second], axis=2)
    buf = jnp.zeros((nb, comps, nz, nx, width, cols), t.dtype)
    buf = lax.dynamic_update_slice(buf, pair[:, :, None], (0, 0, z, 0, 0, 0))
    forward = nz // 2
    backward = nz - 1 - forward
    cur_f = pair
    cur_b = pair
    for k in range(1, forward + 1):
        if k == forward and nz % 2 == 0 and width % 2 == 0:
            half = width // 2
            if hold is not None:
                cur_f, hold = lax.optimization_barrier((cur_f, hold))
                piece = shift(cur_f, "cz", nz, 1)
                buf = lax.dynamic_update_slice(buf, piece[:, :, None], (0, 0, (z - k) % nz, 0, 0, 0))
                break
            a = shift(cur_f[:, :, :, :half], "cz", nz, 1)
            b = shift(cur_b[:, :, :, half:], "cz", nz, -1)
            piece = jnp.concatenate([a, b], axis=3)
            buf = lax.dynamic_update_slice(buf, piece[:, :, None], (0, 0, (z - k) % nz, 0, 0, 0))
            break
        cur_f = shift(cur_f, "cz", nz, 1)
        buf = lax.dynamic_update_slice(buf, cur_f[:, :, None], (0, 0, (z - k) % nz, 0, 0, 0))
        if k <= backward:
            cur_b = shift(cur_b, "cz", nz, -1)
            buf = lax.dynamic_update_slice(buf, cur_b[:, :, None], (0, 0, (z + k) % nz, 0, 0, 0))
    return buf.reshape(nb, comps, nz * nx * width, cols), hold


def shards(stem, branch):
    slab_count = stem.shape[2]
    order_size = stem.shape[3]
    row_count = lax.axis_size("row")
    share = order_size // row_count
    own_t = jnp.swapaxes(branch[0], -1, -2)
    first_t, _ = ring_gather(own_t[:2])

    block = stem[0, 0]
    half_first = right_piece(block, first_t[1]).astype(jnp.bfloat16)
    step_first = left_planar(half_first[0], first_t[0]).astype(jnp.bfloat16)
    second_t, step_first = ring_gather(own_t[2:], hold=step_first)
    outgoing = step_first.reshape(2, row_count, share, order_size)
    moved = lax.all_to_all(outgoing, "row", split_axis=1, concat_axis=1, tiled=True)
    planar = moved.reshape(2, order_size, order_size)
    real_half, imag_half = right_planar(planar, second_t[1])
    step_second = left_halves(
        real_half.astype(jnp.bfloat16), imag_half.astype(jnp.bfloat16), second_t[0]
    ).astype(jnp.bfloat16)
    leaving = step_second.reshape(slab_count, order_size, 2, row_count, share)
    arrived = lax.all_to_all(leaving, "row", split_axis=3, concat_axis=3, tiled=True)
    return arrived.reshape(1, 1, slab_count, order_size, 2, order_size)


def solution(mesh):
    n_col = mesh.shape["col"]
    split = Mesh(mesh.devices.reshape(mesh.shape["row"], n_col // 2, 2), ("row", "cz", "cx"))
    cols = ("cz", "cx")
    placed = (P("row", cols, None, None, None, None), P("row", None, None, None, cols))
    return jax.shard_map(
        shards,
        mesh=split,
        in_specs=placed,
        out_specs=P("row", cols, None, None, None, None),
        check_vma=False,
    )
```

```python
import jax
import jax.numpy as jnp
from jax import lax
from jax.sharding import Mesh
from jax.sharding import PartitionSpec as P


def right_piece(block, piece_t):
    items = block.shape[0]
    order_size = block.shape[1]
    flat = block.reshape(items * order_size, 2 * order_size)
    real_t = piece_t[0]
    imag_t = piece_t[1]
    weight = jnp.block([[real_t, imag_t], [-imag_t, real_t]])
    product = jnp.dot(flat, weight, preferred_element_type=jnp.float32)
    return product.reshape(items, order_size, 2, order_size)


def right_planar(planar, piece_t):
    real_t = piece_t[0]
    imag_t = piece_t[1]
    top = jnp.concatenate([real_t, imag_t], axis=1)
    bottom = jnp.concatenate([-imag_t, real_t], axis=1)
    product = jnp.dot(planar[0], top, preferred_element_type=jnp.float32)
    product = product + jnp.dot(planar[1], bottom, preferred_element_type=jnp.float32)
    cols = piece_t.shape[2]
    return product[:, :cols], product[:, cols:]


def left_planar(block, piece_t):
    real_w = piece_t[0]
    imag_w = piece_t[1]
    weight_real = jnp.concatenate([real_w, imag_w], axis=1)
    weight_imag = jnp.concatenate([-imag_w, real_w], axis=1)
    product = jnp.einsum("ix,ij->xj", weight_real, block[:, 0, :], preferred_element_type=jnp.float32)
    product = product + jnp.einsum(
        "ix,ij->xj", weight_imag, block[:, 1, :], preferred_element_type=jnp.float32
    )
    return product.reshape(2, piece_t.shape[2], block.shape[2])


def left_halves(real_in, imag_in, piece_t):
    rows_out = piece_t.shape[2]
    real_w = piece_t[0]
    imag_w = piece_t[1]
    weight_real = jnp.concatenate([real_w, imag_w], axis=1)
    weight_imag = jnp.concatenate([-imag_w, real_w], axis=1)
    product = jnp.einsum("ix,ij->xj", weight_real, real_in, preferred_element_type=jnp.float32)
    product = product + jnp.einsum(
        "ix,ij->xj", weight_imag, imag_in, preferred_element_type=jnp.float32
    )
    return jnp.stack([product[:rows_out], product[rows_out:]], axis=1)


def left_piece(block, piece_t):
    rows_out = piece_t.shape[2]
    real_in = block[:, :, 0, :]
    imag_in = block[:, :, 1, :]
    real_w = piece_t[0]
    imag_w = piece_t[1]
    weight_real = jnp.concatenate([real_w, imag_w], axis=1)
    weight_imag = jnp.concatenate([-imag_w, real_w], axis=1)
    product = jnp.einsum("ix,eij->exj", weight_real, real_in, preferred_element_type=jnp.float32)
    product = product + jnp.einsum(
        "ix,eij->exj", weight_imag, imag_in, preferred_element_type=jnp.float32
    )
    return jnp.stack([product[:, :rows_out, :], product[:, rows_out:, :]], axis=2)


def shift(x, axis, n, d):
    return lax.ppermute(x, axis, [(i, (i + d) % n) for i in range(n)])


def ring_gather(t, hold=None):
    nz = lax.axis_size("cz")
    nx = lax.axis_size("cx")
    z = lax.axis_index("cz")
    x = lax.axis_index("cx")
    nb, comps, width, cols = t.shape
    other = shift(t, "cx", nx, 1)
    first = jnp.where(x == 0, t, other)
    second = jnp.where(x == 0, other, t)
    pair = jnp.stack([first, second], axis=2)
    buf = jnp.zeros((nb, comps, nz, nx, width, cols), t.dtype)
    buf = lax.dynamic_update_slice(buf, pair[:, :, None], (0, 0, z, 0, 0, 0))
    forward = nz // 2
    backward = nz - 1 - forward
    cur_f = pair
    cur_b = pair
    for k in range(1, forward + 1):
        if k == forward and nz % 2 == 0 and width % 2 == 0:
            half = width // 2
            if hold is not None:
                piece = shift(cur_f, "cz", nz, 1)
                buf = lax.dynamic_update_slice(buf, piece[:, :, None], (0, 0, (z - k) % nz, 0, 0, 0))
                break
            a = shift(cur_f[:, :, :, :half], "cz", nz, 1)
            b = shift(cur_b[:, :, :, half:], "cz", nz, -1)
            piece = jnp.concatenate([a, b], axis=3)
            buf = lax.dynamic_update_slice(buf, piece[:, :, None], (0, 0, (z - k) % nz, 0, 0, 0))
            break
        if hold is not None and k == forward - 1:
            (cur_f, cur_b), hold = lax.optimization_barrier(((cur_f, cur_b), hold))
        cur_f = shift(cur_f, "cz", nz, 1)
        buf = lax.dynamic_update_slice(buf, cur_f[:, :, None], (0, 0, (z - k) % nz, 0, 0, 0))
        if k <= backward:
            cur_b = shift(cur_b, "cz", nz, -1)
            buf = lax.dynamic_update_slice(buf, cur_b[:, :, None], (0, 0, (z + k) % nz, 0, 0, 0))
    return buf.reshape(nb, comps, nz * nx * width, cols), hold


def shards(stem, branch):
    slab_count = stem.shape[2]
    order_size = stem.shape[3]
    row_count = lax.axis_size("row")
    share = order_size // row_count
    own_t = jnp.swapaxes(branch[0], -1, -2)
    first_t, _ = ring_gather(own_t[:2])

    block = stem[0, 0]
    half_first = right_piece(block, first_t[1]).astype(jnp.bfloat16)
    step_first = left_planar(half_first[0], first_t[0]).astype(jnp.bfloat16)
    second_t, step_first = ring_gather(own_t[2:], hold=step_first)
    outgoing = step_first.reshape(2, row_count, share, order_size)
    moved = lax.all_to_all(outgoing, "row", split_axis=1, concat_axis=1, tiled=True)
    planar = moved.reshape(2, order_size, order_size)
    real_half, imag_half = right_planar(planar, second_t[1])
    step_second = left_halves(
        real_half.astype(jnp.bfloat16), imag_half.astype(jnp.bfloat16), second_t[0]
    ).astype(jnp.bfloat16)
    leaving = step_second.reshape(slab_count, order_size, 2, row_count, share)
    arrived = lax.all_to_all(leaving, "row", split_axis=3, concat_axis=3, tiled=True)
    return arrived.reshape(1, 1, slab_count, order_size, 2, order_size)


def solution(mesh):
    n_col = mesh.shape["col"]
    split = Mesh(mesh.devices.reshape(mesh.shape["row"], n_col // 2, 2), ("row", "cz", "cx"))
    cols = ("cz", "cx")
    placed = (P("row", cols, None, None, None, None), P("row", None, None, None, cols))
    return jax.shard_map(
        shards,
        mesh=split,
        in_specs=placed,
        out_specs=P("row", cols, None, None, None, None),
        check_vma=False,
    )
```

```python
import jax
import jax.numpy as jnp
from jax import lax
from jax.sharding import Mesh
from jax.sharding import PartitionSpec as P


def right_piece(block, piece_t):
    items = block.shape[0]
    order_size = block.shape[1]
    flat = block.reshape(items * order_size, 2 * order_size)
    real_t = piece_t[0]
    imag_t = piece_t[1]
    weight = jnp.block([[real_t, imag_t], [-imag_t, real_t]])
    product = jnp.dot(flat, weight, preferred_element_type=jnp.float32)
    return product.reshape(items, order_size, 2, order_size)


def right_planar(planar, piece_t):
    real_t = piece_t[0]
    imag_t = piece_t[1]
    top = jnp.concatenate([real_t, imag_t], axis=1)
    bottom = jnp.concatenate([-imag_t, real_t], axis=1)
    product = jnp.dot(planar[0], top, preferred_element_type=jnp.float32)
    product = product + jnp.dot(planar[1], bottom, preferred_element_type=jnp.float32)
    cols = piece_t.shape[2]
    return product[:, :cols], product[:, cols:]


def left_planar(block, piece_t):
    real_w = piece_t[0]
    imag_w = piece_t[1]
    weight_real = jnp.concatenate([real_w, imag_w], axis=1)
    weight_imag = jnp.concatenate([-imag_w, real_w], axis=1)
    product = jnp.einsum("ix,ij->xj", weight_real, block[:, 0, :], preferred_element_type=jnp.float32)
    product = product + jnp.einsum(
        "ix,ij->xj", weight_imag, block[:, 1, :], preferred_element_type=jnp.float32
    )
    return product.reshape(2, piece_t.shape[2], block.shape[2])


def left_halves(real_in, imag_in, piece_t):
    rows_out = piece_t.shape[2]
    real_w = piece_t[0]
    imag_w = piece_t[1]
    weight_real = jnp.concatenate([real_w, imag_w], axis=1)
    weight_imag = jnp.concatenate([-imag_w, real_w], axis=1)
    product = jnp.einsum("ix,ij->xj", weight_real, real_in, preferred_element_type=jnp.float32)
    product = product + jnp.einsum(
        "ix,ij->xj", weight_imag, imag_in, preferred_element_type=jnp.float32
    )
    return jnp.stack([product[:rows_out], product[rows_out:]], axis=1)


def left_piece(block, piece_t):
    rows_out = piece_t.shape[2]
    real_in = block[:, :, 0, :]
    imag_in = block[:, :, 1, :]
    real_w = piece_t[0]
    imag_w = piece_t[1]
    weight_real = jnp.concatenate([real_w, imag_w], axis=1)
    weight_imag = jnp.concatenate([-imag_w, real_w], axis=1)
    product = jnp.einsum("ix,eij->exj", weight_real, real_in, preferred_element_type=jnp.float32)
    product = product + jnp.einsum(
        "ix,eij->exj", weight_imag, imag_in, preferred_element_type=jnp.float32
    )
    return jnp.stack([product[:, :rows_out, :], product[:, rows_out:, :]], axis=2)


def shift(x, axis, n, d):
    return lax.ppermute(x, axis, [(i, (i + d) % n) for i in range(n)])


def ring_gather(t, hold=None):
    nz = lax.axis_size("cz")
    nx = lax.axis_size("cx")
    z = lax.axis_index("cz")
    x = lax.axis_index("cx")
    nb, comps, width, cols = t.shape
    other = shift(t, "cx", nx, 1)
    first = jnp.where(x == 0, t, other)
    second = jnp.where(x == 0, other, t)
    pair = jnp.stack([first, second], axis=2)
    buf = jnp.zeros((nb, comps, nz, nx, width, cols), t.dtype)
    buf = lax.dynamic_update_slice(buf, pair[:, :, None], (0, 0, z, 0, 0, 0))
    forward = nz // 2
    backward = nz - 1 - forward
    cur_f = pair
    cur_b = pair
    for k in range(1, forward + 1):
        if k == forward and nz % 2 == 0 and width % 2 == 0:
            half = width // 2
            if hold is not None:
                piece = shift(cur_f, "cz", nz, 1)
                buf = lax.dynamic_update_slice(buf, piece[:, :, None], (0, 0, (z - k) % nz, 0, 0, 0))
                break
            a = shift(cur_f[:, :, :, :half], "cz", nz, 1)
            b = shift(cur_b[:, :, :, half:], "cz", nz, -1)
            piece = jnp.concatenate([a, b], axis=3)
            buf = lax.dynamic_update_slice(buf, piece[:, :, None], (0, 0, (z - k) % nz, 0, 0, 0))
            break
        if k <= backward:
            cur_b = shift(cur_b, "cz", nz, -1)
            buf = lax.dynamic_update_slice(buf, cur_b[:, :, None], (0, 0, (z + k) % nz, 0, 0, 0))
        if hold is not None and k == forward - 1:
            cur_f, hold = lax.optimization_barrier((cur_f, hold))
        cur_f = shift(cur_f, "cz", nz, 1)
        buf = lax.dynamic_update_slice(buf, cur_f[:, :, None], (0, 0, (z - k) % nz, 0, 0, 0))
    return buf.reshape(nb, comps, nz * nx * width, cols), hold


def shards(stem, branch):
    slab_count = stem.shape[2]
    order_size = stem.shape[3]
    row_count = lax.axis_size("row")
    share = order_size // row_count
    own_t = jnp.swapaxes(branch[0], -1, -2)
    first_t, _ = ring_gather(own_t[:2])

    block = stem[0, 0]
    half_first = right_piece(block, first_t[1]).astype(jnp.bfloat16)
    step_first = left_planar(half_first[0], first_t[0]).astype(jnp.bfloat16)
    second_t, step_first = ring_gather(own_t[2:], hold=step_first)
    outgoing = step_first.reshape(2, row_count, share, order_size)
    moved = lax.all_to_all(outgoing, "row", split_axis=1, concat_axis=1, tiled=True)
    planar = moved.reshape(2, order_size, order_size)
    real_half, imag_half = right_planar(planar, second_t[1])
    step_second = left_halves(
        real_half.astype(jnp.bfloat16), imag_half.astype(jnp.bfloat16), second_t[0]
    ).astype(jnp.bfloat16)
    leaving = step_second.reshape(slab_count, order_size, 2, row_count, share)
    arrived = lax.all_to_all(leaving, "row", split_axis=3, concat_axis=3, tiled=True)
    return arrived.reshape(1, 1, slab_count, order_size, 2, order_size)


def solution(mesh):
    n_col = mesh.shape["col"]
    split = Mesh(mesh.devices.reshape(mesh.shape["row"], n_col // 2, 2), ("row", "cz", "cx"))
    cols = ("cz", "cx")
    placed = (P("row", cols, None, None, None, None), P("row", None, None, None, cols))
    return jax.shard_map(
        shards,
        mesh=split,
        in_specs=placed,
        out_specs=P("row", cols, None, None, None, None),
        check_vma=False,
    )
```

```python
import jax
import jax.numpy as jnp
from jax import lax
from jax.sharding import Mesh
from jax.sharding import PartitionSpec as P


def right_piece(block, piece_t):
    items = block.shape[0]
    order_size = block.shape[1]
    flat = block.reshape(items * order_size, 2 * order_size)
    real_t = piece_t[0]
    imag_t = piece_t[1]
    weight = jnp.block([[real_t, imag_t], [-imag_t, real_t]])
    product = jnp.dot(flat, weight, preferred_element_type=jnp.float32)
    return product.reshape(items, order_size, 2, order_size)


def right_planar(planar, piece_t):
    real_t = piece_t[0]
    imag_t = piece_t[1]
    top = jnp.concatenate([real_t, imag_t], axis=1)
    bottom = jnp.concatenate([-imag_t, real_t], axis=1)
    product = jnp.dot(planar[0], top, preferred_element_type=jnp.float32)
    product = product + jnp.dot(planar[1], bottom, preferred_element_type=jnp.float32)
    cols = piece_t.shape[2]
    return product[:, :cols], product[:, cols:]


def left_planar(block, piece_t):
    real_w = piece_t[0]
    imag_w = piece_t[1]
    weight_real = jnp.concatenate([real_w, imag_w], axis=1)
    weight_imag = jnp.concatenate([-imag_w, real_w], axis=1)
    product = jnp.einsum("ix,ij->xj", weight_real, block[:, 0, :], preferred_element_type=jnp.float32)
    product = product + jnp.einsum(
        "ix,ij->xj", weight_imag, block[:, 1, :], preferred_element_type=jnp.float32
    )
    return product.reshape(2, piece_t.shape[2], block.shape[2])


def right_grouped(grouped, piece_t):
    real_t = piece_t[0]
    imag_t = piece_t[1]
    top = jnp.concatenate([real_t, imag_t], axis=1)
    bottom = jnp.concatenate([-imag_t, real_t], axis=1)
    weight = jnp.stack([top, bottom], axis=0)
    product = jnp.einsum("pcly,cyk->plk", grouped, weight, preferred_element_type=jnp.float32)
    cols = piece_t.shape[2]
    product = product.reshape(-1, 2 * cols)
    return product[:, :cols], product[:, cols:]


def left_halves(real_in, imag_in, piece_t):
    rows_out = piece_t.shape[2]
    real_w = piece_t[0]
    imag_w = piece_t[1]
    weight_real = jnp.concatenate([real_w, imag_w], axis=1)
    weight_imag = jnp.concatenate([-imag_w, real_w], axis=1)
    product = jnp.einsum("ix,ij->xj", weight_real, real_in, preferred_element_type=jnp.float32)
    product = product + jnp.einsum(
        "ix,ij->xj", weight_imag, imag_in, preferred_element_type=jnp.float32
    )
    return jnp.stack([product[:rows_out], product[rows_out:]], axis=1)


def left_piece(block, piece_t):
    rows_out = piece_t.shape[2]
    real_in = block[:, :, 0, :]
    imag_in = block[:, :, 1, :]
    real_w = piece_t[0]
    imag_w = piece_t[1]
    weight_real = jnp.concatenate([real_w, imag_w], axis=1)
    weight_imag = jnp.concatenate([-imag_w, real_w], axis=1)
    product = jnp.einsum("ix,eij->exj", weight_real, real_in, preferred_element_type=jnp.float32)
    product = product + jnp.einsum(
        "ix,eij->exj", weight_imag, imag_in, preferred_element_type=jnp.float32
    )
    return jnp.stack([product[:, :rows_out, :], product[:, rows_out:, :]], axis=2)


def shift(x, axis, n, d):
    return lax.ppermute(x, axis, [(i, (i + d) % n) for i in range(n)])


def ring_gather(t, hold=None):
    nz = lax.axis_size("cz")
    nx = lax.axis_size("cx")
    z = lax.axis_index("cz")
    x = lax.axis_index("cx")
    nb, comps, width, cols = t.shape
    other = shift(t, "cx", nx, 1)
    first = jnp.where(x == 0, t, other)
    second = jnp.where(x == 0, other, t)
    pair = jnp.stack([first, second], axis=2)
    buf = jnp.zeros((nb, comps, nz, nx, width, cols), t.dtype)
    buf = lax.dynamic_update_slice(buf, pair[:, :, None], (0, 0, z, 0, 0, 0))
    forward = nz // 2
    backward = nz - 1 - forward
    cur_f = pair
    cur_b = pair
    for k in range(1, forward + 1):
        if k == forward and nz % 2 == 0 and width % 2 == 0:
            half = width // 2
            if hold is not None:
                piece = shift(cur_f, "cz", nz, 1)
                buf = lax.dynamic_update_slice(buf, piece[:, :, None], (0, 0, (z - k) % nz, 0, 0, 0))
                break
            a = shift(cur_f[:, :, :, :half], "cz", nz, 1)
            b = shift(cur_b[:, :, :, half:], "cz", nz, -1)
            piece = jnp.concatenate([a, b], axis=3)
            buf = lax.dynamic_update_slice(buf, piece[:, :, None], (0, 0, (z - k) % nz, 0, 0, 0))
            break
        if k <= backward:
            cur_b = shift(cur_b, "cz", nz, -1)
            buf = lax.dynamic_update_slice(buf, cur_b[:, :, None], (0, 0, (z + k) % nz, 0, 0, 0))
        if hold is not None and k == forward - 1:
            cur_f, hold = lax.optimization_barrier((cur_f, hold))
        cur_f = shift(cur_f, "cz", nz, 1)
        buf = lax.dynamic_update_slice(buf, cur_f[:, :, None], (0, 0, (z - k) % nz, 0, 0, 0))
    return buf.reshape(nb, comps, nz * nx * width, cols), hold


def shards(stem, branch):
    slab_count = stem.shape[2]
    order_size = stem.shape[3]
    row_count = lax.axis_size("row")
    share = order_size // row_count
    own_t = jnp.swapaxes(branch[0], -1, -2)
    width = own_t.shape[2]
    left_cols = own_t[0].reshape(2, width, row_count, share).transpose(1, 2, 0, 3)
    right_cols = own_t[1].transpose(1, 0, 2)
    early = jnp.stack([left_cols.reshape(width, -1), right_cols.reshape(width, -1)])
    first_w, _ = ring_gather(early[:, None])
    left_w = first_w[0, 0]
    top = first_w[1, 0]
    bottom = jnp.concatenate([-top[:, order_size:], top[:, :order_size]], axis=1)

    block = stem[0, 0]
    flat = block.reshape(order_size, 2 * order_size)
    weight = jnp.concatenate([top, bottom], axis=0)
    half_first = jnp.dot(flat, weight, preferred_element_type=jnp.float32)
    half_first = half_first.astype(jnp.bfloat16).reshape(order_size, 2, order_size)
    real_slot = (jnp.arange(left_w.shape[1]) % (2 * share)) < share
    left_imag = jnp.where(
        real_slot, -jnp.roll(left_w, -share, axis=1), jnp.roll(left_w, share, axis=1)
    )
    product = jnp.einsum("ix,ij->xj", left_w, half_first[:, 0, :], preferred_element_type=jnp.float32)
    product = product + jnp.einsum(
        "ix,ij->xj", left_imag, half_first[:, 1, :], preferred_element_type=jnp.float32
    )
    step_first = product.astype(jnp.bfloat16).reshape(row_count, 2, share, order_size)
    second_t, step_first = ring_gather(own_t[2:], hold=step_first)
    moved = lax.all_to_all(step_first, "row", split_axis=0, concat_axis=0, tiled=True)
    real_half, imag_half = right_grouped(moved, second_t[1])
    step_second = left_halves(
        real_half.astype(jnp.bfloat16), imag_half.astype(jnp.bfloat16), second_t[0]
    ).astype(jnp.bfloat16)
    leaving = step_second.reshape(slab_count, order_size, 2, row_count, share)
    arrived = lax.all_to_all(leaving, "row", split_axis=3, concat_axis=3, tiled=True)
    return arrived.reshape(1, 1, slab_count, order_size, 2, order_size)


def solution(mesh):
    n_col = mesh.shape["col"]
    split = Mesh(mesh.devices.reshape(mesh.shape["row"], n_col // 2, 2), ("row", "cz", "cx"))
    cols = ("cz", "cx")
    placed = (P("row", cols, None, None, None, None), P("row", None, None, None, cols))
    return jax.shard_map(
        shards,
        mesh=split,
        in_specs=placed,
        out_specs=P("row", cols, None, None, None, None),
        check_vma=False,
    )
```

```python
import jax
import jax.numpy as jnp
from jax import lax
from jax.sharding import Mesh
from jax.sharding import PartitionSpec as P


def right_piece(block, piece_t):
    items = block.shape[0]
    order_size = block.shape[1]
    flat = block.reshape(items * order_size, 2 * order_size)
    real_t = piece_t[0]
    imag_t = piece_t[1]
    weight = jnp.block([[real_t, imag_t], [-imag_t, real_t]])
    product = jnp.dot(flat, weight, preferred_element_type=jnp.float32)
    return product.reshape(items, order_size, 2, order_size)


def right_planar(planar, piece_t):
    real_t = piece_t[0]
    imag_t = piece_t[1]
    top = jnp.concatenate([real_t, imag_t], axis=1)
    bottom = jnp.concatenate([-imag_t, real_t], axis=1)
    product = jnp.dot(planar[0], top, preferred_element_type=jnp.float32)
    product = product + jnp.dot(planar[1], bottom, preferred_element_type=jnp.float32)
    cols = piece_t.shape[2]
    return product[:, :cols], product[:, cols:]


def left_planar(block, piece_t):
    real_w = piece_t[0]
    imag_w = piece_t[1]
    weight_real = jnp.concatenate([real_w, imag_w], axis=1)
    weight_imag = jnp.concatenate([-imag_w, real_w], axis=1)
    product = jnp.einsum("ix,ij->xj", weight_real, block[:, 0, :], preferred_element_type=jnp.float32)
    product = product + jnp.einsum(
        "ix,ij->xj", weight_imag, block[:, 1, :], preferred_element_type=jnp.float32
    )
    return product.reshape(2, piece_t.shape[2], block.shape[2])


def right_grouped(grouped, piece_t):
    real_t = piece_t[0]
    imag_t = piece_t[1]
    top = jnp.concatenate([real_t, imag_t], axis=1)
    bottom = jnp.concatenate([-imag_t, real_t], axis=1)
    weight = jnp.stack([top, bottom], axis=0)
    product = jnp.einsum("pcly,cyk->plk", grouped, weight, preferred_element_type=jnp.float32)
    cols = piece_t.shape[2]
    product = product.reshape(-1, 2 * cols)
    return product[:, :cols], product[:, cols:]


def left_halves(real_in, imag_in, piece_t):
    rows_out = piece_t.shape[2]
    real_w = piece_t[0]
    imag_w = piece_t[1]
    weight_real = jnp.concatenate([real_w, imag_w], axis=1)
    weight_imag = jnp.concatenate([-imag_w, real_w], axis=1)
    product = jnp.einsum("ix,ij->xj", weight_real, real_in, preferred_element_type=jnp.float32)
    product = product + jnp.einsum(
        "ix,ij->xj", weight_imag, imag_in, preferred_element_type=jnp.float32
    )
    return jnp.stack([product[:rows_out], product[rows_out:]], axis=1)


def left_piece(block, piece_t):
    rows_out = piece_t.shape[2]
    real_in = block[:, :, 0, :]
    imag_in = block[:, :, 1, :]
    real_w = piece_t[0]
    imag_w = piece_t[1]
    weight_real = jnp.concatenate([real_w, imag_w], axis=1)
    weight_imag = jnp.concatenate([-imag_w, real_w], axis=1)
    product = jnp.einsum("ix,eij->exj", weight_real, real_in, preferred_element_type=jnp.float32)
    product = product + jnp.einsum(
        "ix,eij->exj", weight_imag, imag_in, preferred_element_type=jnp.float32
    )
    return jnp.stack([product[:, :rows_out, :], product[:, rows_out:, :]], axis=2)


def shift(x, axis, n, d):
    return lax.ppermute(x, axis, [(i, (i + d) % n) for i in range(n)])


def ring_gather(t, hold=None):
    nz = lax.axis_size("cz")
    nx = lax.axis_size("cx")
    z = lax.axis_index("cz")
    x = lax.axis_index("cx")
    nb, comps, width, cols = t.shape
    other = shift(t, "cx", nx, 1)
    first = jnp.where(x == 0, t, other)
    second = jnp.where(x == 0, other, t)
    pair = jnp.stack([first, second], axis=2)
    buf = jnp.zeros((nb, comps, nz, nx, width, cols), t.dtype)
    buf = lax.dynamic_update_slice(buf, pair[:, :, None], (0, 0, z, 0, 0, 0))
    forward = nz // 2
    backward = nz - 1 - forward
    cur_f = pair
    cur_b = pair
    for k in range(1, forward + 1):
        if k == forward and nz % 2 == 0 and width % 2 == 0:
            half = width // 2
            if hold is not None:
                cur_f, hold = lax.optimization_barrier((cur_f, hold))
                piece = shift(cur_f, "cz", nz, 1)
                buf = lax.dynamic_update_slice(buf, piece[:, :, None], (0, 0, (z - k) % nz, 0, 0, 0))
                break
            a = shift(cur_f[:, :, :, :half], "cz", nz, 1)
            b = shift(cur_b[:, :, :, half:], "cz", nz, -1)
            piece = jnp.concatenate([a, b], axis=3)
            buf = lax.dynamic_update_slice(buf, piece[:, :, None], (0, 0, (z - k) % nz, 0, 0, 0))
            break
        if k <= backward:
            cur_b = shift(cur_b, "cz", nz, -1)
            buf = lax.dynamic_update_slice(buf, cur_b[:, :, None], (0, 0, (z + k) % nz, 0, 0, 0))
        cur_f = shift(cur_f, "cz", nz, 1)
        buf = lax.dynamic_update_slice(buf, cur_f[:, :, None], (0, 0, (z - k) % nz, 0, 0, 0))
    return buf.reshape(nb, comps, nz * nx * width, cols), hold


def shards(stem, branch):
    slab_count = stem.shape[2]
    order_size = stem.shape[3]
    row_count = lax.axis_size("row")
    share = order_size // row_count
    own_t = jnp.swapaxes(branch[0], -1, -2)
    width = own_t.shape[2]
    left_cols = own_t[0].reshape(2, width, row_count, share).transpose(1, 2, 0, 3)
    right_cols = own_t[1].transpose(1, 0, 2)
    early = jnp.stack([left_cols.reshape(width, -1), right_cols.reshape(width, -1)])
    first_w, _ = ring_gather(early[:, None])
    left_w = first_w[0, 0]
    top = first_w[1, 0]
    bottom = jnp.concatenate([-top[:, order_size:], top[:, :order_size]], axis=1)

    block = stem[0, 0]
    flat = block.reshape(order_size, 2 * order_size)
    weight = jnp.concatenate([top, bottom], axis=0)
    half_first = jnp.dot(flat, weight, preferred_element_type=jnp.float32)
    half_first = half_first.astype(jnp.bfloat16).reshape(order_size, 2, order_size)
    real_slot = (jnp.arange(left_w.shape[1]) % (2 * share)) < share
    left_imag = jnp.where(
        real_slot, -jnp.roll(left_w, -share, axis=1), jnp.roll(left_w, share, axis=1)
    )
    product = jnp.einsum("ix,ij->xj", left_w, half_first[:, 0, :], preferred_element_type=jnp.float32)
    product = product + jnp.einsum(
        "ix,ij->xj", left_imag, half_first[:, 1, :], preferred_element_type=jnp.float32
    )
    step_first = product.astype(jnp.bfloat16).reshape(row_count, 2, share, order_size)
    second_t, step_first = ring_gather(own_t[2:], hold=step_first)
    moved = lax.all_to_all(step_first, "row", split_axis=0, concat_axis=0, tiled=True)
    real_half, imag_half = right_grouped(moved, second_t[1])
    step_second = left_halves(
        real_half.astype(jnp.bfloat16), imag_half.astype(jnp.bfloat16), second_t[0]
    ).astype(jnp.bfloat16)
    leaving = step_second.reshape(slab_count, order_size, 2, row_count, share)
    arrived = lax.all_to_all(leaving, "row", split_axis=3, concat_axis=3, tiled=True)
    return arrived.reshape(1, 1, slab_count, order_size, 2, order_size)


def solution(mesh):
    n_col = mesh.shape["col"]
    split = Mesh(mesh.devices.reshape(mesh.shape["row"], n_col // 2, 2), ("row", "cz", "cx"))
    cols = ("cz", "cx")
    placed = (P("row", cols, None, None, None, None), P("row", None, None, None, cols))
    return jax.shard_map(
        shards,
        mesh=split,
        in_specs=placed,
        out_specs=P("row", cols, None, None, None, None),
        check_vma=False,
    )
```

```python
import jax
import jax.numpy as jnp
from jax import lax
from jax.sharding import Mesh
from jax.sharding import PartitionSpec as P


def right_piece(block, piece_t):
    items = block.shape[0]
    order_size = block.shape[1]
    flat = block.reshape(items * order_size, 2 * order_size)
    real_t = piece_t[0]
    imag_t = piece_t[1]
    weight = jnp.block([[real_t, imag_t], [-imag_t, real_t]])
    product = jnp.dot(flat, weight, preferred_element_type=jnp.float32)
    return product.reshape(items, order_size, 2, order_size)


def right_planar(planar, piece_t):
    real_t = piece_t[0]
    imag_t = piece_t[1]
    top = jnp.concatenate([real_t, imag_t], axis=1)
    bottom = jnp.concatenate([-imag_t, real_t], axis=1)
    product = jnp.dot(planar[0], top, preferred_element_type=jnp.float32)
    product = product + jnp.dot(planar[1], bottom, preferred_element_type=jnp.float32)
    cols = piece_t.shape[2]
    return product[:, :cols], product[:, cols:]


def left_planar(block, piece_t):
    real_w = piece_t[0]
    imag_w = piece_t[1]
    weight_real = jnp.concatenate([real_w, imag_w], axis=1)
    weight_imag = jnp.concatenate([-imag_w, real_w], axis=1)
    product = jnp.einsum("ix,ij->xj", weight_real, block[:, 0, :], preferred_element_type=jnp.float32)
    product = product + jnp.einsum(
        "ix,ij->xj", weight_imag, block[:, 1, :], preferred_element_type=jnp.float32
    )
    return product.reshape(2, piece_t.shape[2], block.shape[2])


def left_halves(real_in, imag_in, piece_t):
    rows_out = piece_t.shape[2]
    real_w = piece_t[0]
    imag_w = piece_t[1]
    weight_real = jnp.concatenate([real_w, imag_w], axis=1)
    weight_imag = jnp.concatenate([-imag_w, real_w], axis=1)
    product = jnp.einsum("ix,ij->xj", weight_real, real_in, preferred_element_type=jnp.float32)
    product = product + jnp.einsum(
        "ix,ij->xj", weight_imag, imag_in, preferred_element_type=jnp.float32
    )
    return jnp.stack([product[:rows_out], product[rows_out:]], axis=1)


def left_piece(block, piece_t):
    rows_out = piece_t.shape[2]
    real_in = block[:, :, 0, :]
    imag_in = block[:, :, 1, :]
    real_w = piece_t[0]
    imag_w = piece_t[1]
    weight_real = jnp.concatenate([real_w, imag_w], axis=1)
    weight_imag = jnp.concatenate([-imag_w, real_w], axis=1)
    product = jnp.einsum("ix,eij->exj", weight_real, real_in, preferred_element_type=jnp.float32)
    product = product + jnp.einsum(
        "ix,eij->exj", weight_imag, imag_in, preferred_element_type=jnp.float32
    )
    return jnp.stack([product[:, :rows_out, :], product[:, rows_out:, :]], axis=2)


def shift(x, axis, n, d):
    return lax.ppermute(x, axis, [(i, (i + d) % n) for i in range(n)])


def ring_gather(t, hold=None):
    nz = lax.axis_size("cz")
    nx = lax.axis_size("cx")
    z = lax.axis_index("cz")
    x = lax.axis_index("cx")
    nb, comps, width, cols = t.shape
    other = shift(t, "cx", nx, 1)
    first = jnp.where(x == 0, t, other)
    second = jnp.where(x == 0, other, t)
    pair = jnp.stack([first, second], axis=2)
    pieces = {0: pair}
    buf = jnp.zeros((nb, comps, nz, nx, width, cols), t.dtype)

    def put(buf, piece, offset):
        if hold is not None:
            pieces[offset % nz] = piece
            return buf
        return lax.dynamic_update_slice(buf, piece[:, :, None], (0, 0, (z + offset) % nz, 0, 0, 0))

    buf = put(buf, pair, 0)
    forward = nz // 2
    backward = nz - 1 - forward
    cur_f = pair
    cur_b = pair
    for k in range(1, forward + 1):
        if k == forward and nz % 2 == 0 and width % 2 == 0:
            half = width // 2
            if hold is not None:
                buf = put(buf, shift(cur_f, "cz", nz, 1), -k)
                break
            a = shift(cur_f[:, :, :, :half], "cz", nz, 1)
            b = shift(cur_b[:, :, :, half:], "cz", nz, -1)
            buf = put(buf, jnp.concatenate([a, b], axis=3), -k)
            break
        if k <= backward:
            cur_b = shift(cur_b, "cz", nz, -1)
            buf = put(buf, cur_b, k)
        if hold is not None and k == forward - 1:
            cur_f, hold = lax.optimization_barrier((cur_f, hold))
        cur_f = shift(cur_f, "cz", nz, 1)
        buf = put(buf, cur_f, -k)
    if hold is not None:
        relative = jnp.stack([pieces[o] for o in range(nz)], axis=2)
        twice = jnp.concatenate([relative, relative], axis=2)
        buf = lax.dynamic_slice_in_dim(twice, (nz - z) % nz, nz, axis=2)
    return buf.reshape(nb, comps, nz * nx * width, cols), hold


def shards(stem, branch):
    slab_count = stem.shape[2]
    order_size = stem.shape[3]
    row_count = lax.axis_size("row")
    share = order_size // row_count
    own_t = jnp.swapaxes(branch[0], -1, -2)
    first_t, _ = ring_gather(own_t[:2])

    block = stem[0, 0]
    half_first = right_piece(block, first_t[1]).astype(jnp.bfloat16)
    step_first = left_planar(half_first[0], first_t[0]).astype(jnp.bfloat16)
    second_t, step_first = ring_gather(own_t[2:], hold=step_first)
    outgoing = step_first.reshape(2, row_count, share, order_size)
    moved = lax.all_to_all(outgoing, "row", split_axis=1, concat_axis=1, tiled=True)
    planar = moved.reshape(2, order_size, order_size)
    real_half, imag_half = right_planar(planar, second_t[1])
    step_second = left_halves(
        real_half.astype(jnp.bfloat16), imag_half.astype(jnp.bfloat16), second_t[0]
    ).astype(jnp.bfloat16)
    leaving = step_second.reshape(slab_count, order_size, 2, row_count, share)
    arrived = lax.all_to_all(leaving, "row", split_axis=3, concat_axis=3, tiled=True)
    return arrived.reshape(1, 1, slab_count, order_size, 2, order_size)


def solution(mesh):
    n_col = mesh.shape["col"]
    split = Mesh(mesh.devices.reshape(mesh.shape["row"], n_col // 2, 2), ("row", "cz", "cx"))
    cols = ("cz", "cx")
    placed = (P("row", cols, None, None, None, None), P("row", None, None, None, cols))
    return jax.shard_map(
        shards,
        mesh=split,
        in_specs=placed,
        out_specs=P("row", cols, None, None, None, None),
        check_vma=False,
    )
```
